1024 devices in a mesh: segment: 8 (over y), ctx: 16 (over z), tp: 8 (over x, core).
Axes of the slice: x: 4, y: 8, z: 16, core: 2. Of those that a mesh axis runs over, the one named last changes fastest.
Arguments:
- query: bfloat16 [8, 2048, 8192], P('segment', 'ctx', 'tp'), may hold values from -150 to 150
- keys: bfloat16 [8, 2048, 1024], P('segment', 'ctx', 'tp'), may hold values from -6 to 6
- values: bfloat16 [8, 2048, 1024], P('segment', 'ctx', 'tp'), may hold values from -6 to 6
- attn_out: bfloat16 [8, 2048, 8192], P('segment', 'ctx', 'tp'), may hold values from -4 to 4
- grad_out: bfloat16 [8, 2048, 8192], P('segment', ('ctx', 'tp')), may hold values from -6 to 6
- block_of: int32 [8, 32], P('segment'), may hold values from 0 to 31, each once within a row
Outputs:
- grad_query: bfloat16 [8, 2048, 8192], P('segment', 'ctx', 'tp')
- grad_keys: bfloat16 [8, 2048, 1024], P('segment', 'ctx', 'tp')
- grad_values: bfloat16 [8, 2048, 1024], P('segment', 'ctx', 'tp')
The draws below stay inside these ranges and needn't reach their ends.
All inputs are finite; a program needn't handle non-finite values.
Results may differ from the reference program's by a relative error of at most 0.0055.
Values may be sent and summed in bfloat16 or wider, within the bound.
No kernel may reach another device: no remote copies, remote signals or barrier semaphores. Data moves between devices by JAX's collectives and lax.ppermute only.
A program may use at most 32 MiB of HBM per device.

```python
import jax
import jax.numpy as jnp
from jax import lax

HEADS = 64
KV_HEADS = 8
HEAD_DIM = 128
ROWS = 128
SEQ = 2048
N_SEGMENT = 8
N_CTX = 16


def draw_query(key, part):
    shape = (N_SEGMENT, SEQ, HEADS * HEAD_DIM)
    base = jnp.clip(jax.random.normal(jax.random.fold_in(key, 11), shape, jnp.float32), -6.0, 6.0)
    return base.astype(jnp.bfloat16)


def steps_of(stream_key, shape, shards, least, top_value):
    level = 1.0
    for position, shards_of in shards:
        heights = jax.random.uniform(jax.random.fold_in(jax.random.fold_in(stream_key, 6), position), (shards_of,), jnp.float32, least / len(shards), top_value / len(shards))
        level = level * jnp.repeat(jnp.exp(heights), shape[position] // shards_of).reshape((-1,) + (1,) * (len(shape) - 1 - position))
    return level


def normal_values(stream_key, shape, spread, bound, cuts=(), held_as=jnp.bfloat16):
    values = spread * jax.random.normal(stream_key, shape, jnp.float32)
    if cuts:
        values = values * steps_of(stream_key, shape, cuts, -0.22, 0.18)
    return jnp.clip(values, -bound, bound).astype(held_as)


def setup_inputs(seed: int = 0) -> dict:
    arg_keys = jax.random.split(jax.random.key(seed), 7)
    return {
        "query": draw_query(jax.random.fold_in(arg_keys[6], 71), 0),
        "keys": normal_values(arg_keys[1], (N_SEGMENT, SEQ, KV_HEADS * HEAD_DIM), 1.0, 6.0, ((0, 8), (1, 16), (2, 8))),
        "values": normal_values(arg_keys[2], (N_SEGMENT, SEQ, KV_HEADS * HEAD_DIM), 1.0, 6.0, ((0, 8), (1, 16), (2, 8))),
        "attn_out": normal_values(arg_keys[3], (N_SEGMENT, SEQ, HEADS * HEAD_DIM), 0.3, 4.0, ((0, 8), (1, 16), (2, 8))),
        "grad_out": normal_values(arg_keys[4], (N_SEGMENT, SEQ, HEADS * HEAD_DIM), 1.0, 6.0, ((0, 8), (1, 128))),
        "block_of": jax.vmap(lambda own: jax.random.permutation(own, 2 * N_CTX))(jax.random.split(arg_keys[5], N_SEGMENT)).reshape((N_SEGMENT, 2 * N_CTX)).astype(jnp.int32),
    }


HIGH = lax.Precision.HIGHEST


def positions(order_row):
    half = ROWS // 2
    rows = jnp.arange(SEQ, dtype=jnp.int32)
    return order_row[rows // half] * half + rows % half


def rounded(value):
    return lax.optimization_barrier(value.astype(jnp.bfloat16)).astype(jnp.float32)


def attention_section(inputs):
    query, keys, values, attn_out, grad_out, order_row = inputs
    per = HEADS // KV_HEADS
    scale = HEAD_DIM ** -0.5
    pos = positions(order_row)
    allowed = pos[None, :] <= pos[:, None]
    q_all = query.reshape(SEQ, KV_HEADS, per, HEAD_DIM).transpose(1, 0, 2, 3)
    o_all = attn_out.reshape(SEQ, KV_HEADS, per, HEAD_DIM).transpose(1, 0, 2, 3)
    do_all = grad_out.reshape(SEQ, KV_HEADS, per, HEAD_DIM).transpose(1, 0, 2, 3)
    k_all = keys.reshape(SEQ, KV_HEADS, HEAD_DIM).transpose(1, 0, 2)
    v_all = values.reshape(SEQ, KV_HEADS, HEAD_DIM).transpose(1, 0, 2)

    def one_group(group):
        q_g, o_g, do_g, k_g, v_g = group
        qf = q_g.astype(jnp.float32)
        dof = do_g.astype(jnp.float32)
        kf = k_g.astype(jnp.float32)
        vf = v_g.astype(jnp.float32)
        scores = scale * jnp.einsum("ied,jd->eij", qf, kf, precision=HIGH)
        lse = jax.nn.logsumexp(jnp.where(allowed[None], scores, -jnp.inf), axis=-1)
        prob = jnp.where(allowed[None], jnp.exp(scores - lse[:, :, None]), 0.0)
        prob_b = rounded(prob)
        delta = jnp.sum(o_g.astype(jnp.float32) * dof, axis=-1).T
        dvalue = jnp.einsum("eij,ied->jd", prob_b, dof, precision=HIGH)
        dprob = jnp.einsum("ied,jd->eij", dof, vf, precision=HIGH)
        dscore = rounded(prob * (dprob - delta[:, :, None]))
        dquery = scale * jnp.einsum("eij,jd->ied", dscore, kf, precision=HIGH)
        dkey = scale * jnp.einsum("eij,ied->jd", dscore, qf, precision=HIGH)
        return dquery.astype(jnp.bfloat16), dkey.astype(jnp.bfloat16), dvalue.astype(jnp.bfloat16)

    dq, dk, dv = lax.map(one_group, (q_all, o_all, do_all, k_all, v_all))
    dq = dq.transpose(1, 0, 2, 3).reshape(SEQ, HEADS * HEAD_DIM)
    dk = dk.transpose(1, 0, 2).reshape(SEQ, KV_HEADS * HEAD_DIM)
    dv = dv.transpose(1, 0, 2).reshape(SEQ, KV_HEADS * HEAD_DIM)
    return dq, dk, dv


def reference(query, keys, values, attn_out, grad_out, block_of):
    incoming = jnp.roll(grad_out, -1, axis=0)
    grad_query, grad_keys, grad_values = lax.map(attention_section, (query, keys, values, attn_out, incoming, block_of))
    return grad_query, grad_keys, grad_values
```

```python
import jax
import jax.numpy as jnp
from jax import lax
from jax.sharding import PartitionSpec as P

HEAD_DIM = 128
CHUNKS = 4


def passed_along(value, axis, steps):
    count = lax.axis_size(axis)
    pairs = [(source, (source + steps) % count) for source in range(count)]
    return lax.ppermute(value, axis, pairs)


def body(query, keys, values, attn_out, grad_out, block_of):
    rows = query.shape[1]
    kv_width = keys.shape[2]
    head_dim = HEAD_DIM
    groups = kv_width // head_dim
    heads = query.shape[2] // head_dim
    per = heads // groups
    scale = head_dim ** (-0.5)
    half = rows // 2
    order = block_of[0]
    me = lax.axis_index("ctx")
    handed = passed_along(grad_out[0], "segment", -1)
    incoming = lax.all_to_all(handed, "tp", split_axis=1, concat_axis=0, tiled=True)
    q_local = query[0].reshape(rows, groups, per, head_dim)
    do_local = incoming.reshape(rows, groups, per, head_dim)
    delta = jnp.sum(
        attn_out[0].reshape(rows, groups, per, head_dim).astype(jnp.float32)
        * do_local.astype(jnp.float32),
        axis=-1,
    )
    delta = jnp.transpose(delta, (1, 2, 0))

    def place(first, length):
        index = first + jnp.arange(length, dtype=jnp.int32)
        table = (index // half)[:, None] == jnp.arange(order.shape[0], dtype=jnp.int32)[None, :]
        return jnp.sum(jnp.where(table, order[None, :], 0), axis=1) * half + index % half

    q_pos = place(me * rows, rows)

    kv = jnp.concatenate([keys[0], values[0]], axis=1)
    kv_all = lax.all_gather(kv, "ctx", axis=0, tiled=True)
    seq = kv_all.shape[0]
    k_all = kv_all[:, :kv_width].reshape(seq, groups, head_dim)
    v_all = kv_all[:, kv_width:].reshape(seq, groups, head_dim)
    k_pos_all = place(jnp.int32(0), seq)
    width = seq // CHUNKS

    def chunk_scores(c):
        k_c = k_all[c * width:(c + 1) * width]
        scores = scale * jnp.einsum(
            "iged,jgd->geij", q_local, k_c, preferred_element_type=jnp.float32
        )
        allowed = k_pos_all[c * width:(c + 1) * width][None, :] <= q_pos[:, None]
        return scores, allowed

    tops = []
    for c in range(CHUNKS):
        scores, allowed = chunk_scores(c)
        tops.append(jnp.max(jnp.where(allowed, scores, -1e30), axis=-1))
    top = tops[0]
    for t in tops[1:]:
        top = jnp.maximum(top, t)
    total = jnp.zeros_like(top)
    for c in range(CHUNKS):
        scores, allowed = chunk_scores(c)
        total = total + jnp.sum(jnp.where(allowed, jnp.exp(scores - top[..., None]), 0.0), axis=-1)
    lse = top + jnp.log(total)

    dquery = jnp.zeros((rows, groups, per, head_dim), jnp.float32)
    dks = []
    dvs = []
    for c in range(CHUNKS):
        scores, allowed = chunk_scores(c)
        k_c = k_all[c * width:(c + 1) * width]
        v_c = v_all[c * width:(c + 1) * width]
        prob = jnp.where(allowed, jnp.exp(scores - lse[..., None]), 0.0)
        prob_b = prob.astype(jnp.bfloat16)
        dvalue = jnp.einsum("geij,iged->jgd", prob_b, do_local, preferred_element_type=jnp.float32)
        dprob = jnp.einsum("iged,jgd->geij", do_local, v_c, preferred_element_type=jnp.float32)
        dscore = (prob * (dprob - delta[..., None])).astype(jnp.bfloat16)
        dquery = dquery + jnp.einsum("geij,jgd->iged", dscore, k_c, preferred_element_type=jnp.float32)
        dkey = jnp.einsum("geij,iged->jgd", dscore, q_local, preferred_element_type=jnp.float32)
        dks.append(dkey.reshape(width, kv_width))
        dvs.append(dvalue.reshape(width, kv_width))
    dkv = jnp.concatenate([jnp.concatenate(dks, axis=0), jnp.concatenate(dvs, axis=0)], axis=1)
    dkv = lax.psum_scatter(dkv, "ctx", scatter_dimension=0, tiled=True)
    dkey = dkv[:, :kv_width]
    dvalue = dkv[:, kv_width:]
    grad_query = (scale * dquery).reshape(rows, heads * head_dim).astype(jnp.bfloat16)[None]
    grad_keys = (scale * dkey).astype(jnp.bfloat16)[None]
    grad_values = dvalue.astype(jnp.bfloat16)[None]
    return (grad_query, grad_keys, grad_values)


def solution(mesh):
    return jax.shard_map(
        body,
        mesh=mesh,
        in_specs=(
            P("segment", "ctx", "tp"),
            P("segment", "ctx", "tp"),
            P("segment", "ctx", "tp"),
            P("segment", "ctx", "tp"),
            P("segment", ("ctx", "tp"), None),
            P("segment", None),
        ),
        out_specs=(P("segment", "ctx", "tp"), P("segment", "ctx", "tp"), P("segment", "ctx", "tp")),
        check_vma=False,
    )
```

```python
import jax
import jax.numpy as jnp
from jax import lax
from jax.sharding import PartitionSpec as P

HEAD_DIM = 128
CHUNKS = 4


def passed_along(value, axis, steps):
    count = lax.axis_size(axis)
    pairs = [(source, (source + steps) % count) for source in range(count)]
    return lax.ppermute(value, axis, pairs)


def body(query, keys, values, attn_out, grad_out, block_of):
    rows = query.shape[1]
    kv_width = keys.shape[2]
    head_dim = HEAD_DIM
    groups = kv_width // head_dim
    heads = query.shape[2] // head_dim
    per = heads // groups
    scale = head_dim ** (-0.5)
    half = rows // 2
    order = block_of[0]
    me = lax.axis_index("ctx")
    handed = passed_along(grad_out[0], "segment", -1)
    incoming = lax.all_to_all(handed, "tp", split_axis=1, concat_axis=0, tiled=True)
    q_local = query[0].reshape(rows, groups, per, head_dim)
    do_local = incoming.reshape(rows, groups, per, head_dim)
    delta = jnp.sum(
        attn_out[0].reshape(rows, groups, per, head_dim).astype(jnp.float32)
        * do_local.astype(jnp.float32),
        axis=-1,
    )
    delta = jnp.transpose(delta, (1, 2, 0))

    def place(first, length):
        index = first + jnp.arange(length, dtype=jnp.int32)
        table = (index // half)[:, None] == jnp.arange(order.shape[0], dtype=jnp.int32)[None, :]
        return jnp.sum(jnp.where(table, order[None, :], 0), axis=1) * half + index % half

    q_pos = place(me * rows, rows)

    kv = jnp.concatenate([keys[0], values[0]], axis=1)
    count = lax.axis_size("ctx")
    reach = count // 2
    slots = [None] * count
    slots[reach] = kv
    right = kv
    left = kv
    for step in range(1, reach + 1):
        right = passed_along(right, "ctx", 1)
        slots[reach - step] = right
        if step < count - reach:
            left = passed_along(left, "ctx", -1)
            slots[reach + step] = left
    kv_all = jnp.concatenate(slots, axis=0)
    seq = kv_all.shape[0]
    k_all = kv_all[:, :kv_width].reshape(seq, groups, head_dim)
    v_all = kv_all[:, kv_width:].reshape(seq, groups, head_dim)
    slot_rows = jnp.arange(seq, dtype=jnp.int32)
    global_rows = ((me + slot_rows // rows - reach) % count) * rows + slot_rows % rows
    k_pos_all = jnp.take(order, global_rows // half) * half + global_rows % half
    width = seq // CHUNKS

    def chunk_scores(c):
        k_c = k_all[c * width:(c + 1) * width]
        scores = scale * jnp.einsum(
            "iged,jgd->geij", q_local, k_c, preferred_element_type=jnp.float32
        )
        allowed = k_pos_all[c * width:(c + 1) * width][None, :] <= q_pos[:, None]
        return scores, allowed

    tops = []
    for c in range(CHUNKS):
        scores, allowed = chunk_scores(c)
        tops.append(jnp.max(jnp.where(allowed, scores, -1e30), axis=-1))
    top = tops[0]
    for t in tops[1:]:
        top = jnp.maximum(top, t)
    total = jnp.zeros_like(top)
    for c in range(CHUNKS):
        scores, allowed = chunk_scores(c)
        total = total + jnp.sum(jnp.where(allowed, jnp.exp(scores - top[..., None]), 0.0), axis=-1)
    lse = top + jnp.log(total)

    dquery = jnp.zeros((rows, groups, per, head_dim), jnp.float32)
    dks = []
    dvs = []
    for c in range(CHUNKS):
        scores, allowed = chunk_scores(c)
        k_c = k_all[c * width:(c + 1) * width]
        v_c = v_all[c * width:(c + 1) * width]
        prob = jnp.where(allowed, jnp.exp(scores - lse[..., None]), 0.0)
        prob_b = prob.astype(jnp.bfloat16)
        dvalue = jnp.einsum("geij,iged->jgd", prob_b, do_local, preferred_element_type=jnp.float32)
        dprob = jnp.einsum("iged,jgd->geij", do_local, v_c, preferred_element_type=jnp.float32)
        dscore = (prob * (dprob - delta[..., None])).astype(jnp.bfloat16)
        dquery = dquery + jnp.einsum("geij,jgd->iged", dscore, k_c, preferred_element_type=jnp.float32)
        dkey = jnp.einsum("geij,iged->jgd", dscore, q_local, preferred_element_type=jnp.float32)
        dks.append(dkey.reshape(width, kv_width))
        dvs.append(dvalue.reshape(width, kv_width))
    parts = [jnp.concatenate([dk_c, dv_c], axis=1) for dk_c, dv_c in zip(dks, dvs)]
    parts = jnp.concatenate(parts, axis=0).reshape(count, rows, 2 * kv_width)
    going_left = parts[0]
    for step in range(1, reach):
        going_left = passed_along(going_left, "ctx", -1) + parts[step]
    going_left = passed_along(going_left, "ctx", -1)
    dkv = parts[reach] + going_left
    if count - reach > 1:
        going_right = parts[count - 1]
        for step in range(1, count - reach - 1):
            going_right = passed_along(going_right, "ctx", 1) + parts[count - 1 - step]
        dkv = dkv + passed_along(going_right, "ctx", 1)
    dkey = dkv[:, :kv_width]
    dvalue = dkv[:, kv_width:]
    grad_query = (scale * dquery).reshape(rows, heads * head_dim).astype(jnp.bfloat16)[None]
    grad_keys = (scale * dkey).astype(jnp.bfloat16)[None]
    grad_values = dvalue.astype(jnp.bfloat16)[None]
    return (grad_query, grad_keys, grad_values)


def solution(mesh):
    return jax.shard_map(
        body,
        mesh=mesh,
        in_specs=(
            P("segment", "ctx", "tp"),
            P("segment", "ctx", "tp"),
            P("segment", "ctx", "tp"),
            P("segment", "ctx", "tp"),
            P("segment", ("ctx", "tp"), None),
            P("segment", None),
        ),
        out_specs=(P("segment", "ctx", "tp"), P("segment", "ctx", "tp"), P("segment", "ctx", "tp")),
        check_vma=False,
    )
```

```python
import jax
import jax.numpy as jnp
from jax import lax
from jax.sharding import PartitionSpec as P

HEAD_DIM = 128
CHUNKS = 4


def passed_along(value, axis, steps):
    count = lax.axis_size(axis)
    pairs = [(source, (source + steps) % count) for source in range(count)]
    return lax.ppermute(value, axis, pairs)


def body(query, keys, values, attn_out, grad_out, block_of):
    rows = query.shape[1]
    kv_width = keys.shape[2]
    head_dim = HEAD_DIM
    groups = kv_width // head_dim
    heads = query.shape[2] // head_dim
    per = heads // groups
    scale = head_dim ** (-0.5)
    half = rows // 2
    order = block_of[0]
    me = lax.axis_index("ctx")
    handed = passed_along(grad_out[0], "segment", -1)
    incoming = lax.all_to_all(handed, "tp", split_axis=1, concat_axis=0, tiled=True)
    q_local = query[0].reshape(rows, groups, per, head_dim)
    do_local = incoming.reshape(rows, groups, per, head_dim)
    delta = jnp.sum(
        attn_out[0].reshape(rows, groups, per, head_dim).astype(jnp.float32)
        * do_local.astype(jnp.float32),
        axis=-1,
    )
    delta = jnp.transpose(delta, (1, 2, 0))

    def place(first, length):
        index = first + jnp.arange(length, dtype=jnp.int32)
        table = (index // half)[:, None] == jnp.arange(order.shape[0], dtype=jnp.int32)[None, :]
        return jnp.sum(jnp.where(table, order[None, :], 0), axis=1) * half + index % half

    q_pos = place(me * rows, rows)

    kv = jnp.concatenate([keys[0], values[0]], axis=1)
    count = lax.axis_size("ctx")
    kv_all = lax.all_to_all(
        jnp.broadcast_to(kv[None], (count,) + kv.shape), "ctx", 0, 0, tiled=True
    ).reshape(count * rows, 2 * kv_width)
    seq = kv_all.shape[0]
    k_all = kv_all[:, :kv_width].reshape(seq, groups, head_dim)
    v_all = kv_all[:, kv_width:].reshape(seq, groups, head_dim)
    k_pos_all = place(jnp.int32(0), seq)
    width = seq // CHUNKS

    def chunk_scores(c):
        k_c = k_all[c * width:(c + 1) * width]
        scores = scale * jnp.einsum(
            "iged,jgd->geij", q_local, k_c, preferred_element_type=jnp.float32
        )
        allowed = k_pos_all[c * width:(c + 1) * width][None, :] <= q_pos[:, None]
        return scores, allowed

    tops = []
    for c in range(CHUNKS):
        scores, allowed = chunk_scores(c)
        tops.append(jnp.max(jnp.where(allowed, scores, -1e30), axis=-1))
    top = tops[0]
    for t in tops[1:]:
        top = jnp.maximum(top, t)
    total = jnp.zeros_like(top)
    for c in range(CHUNKS):
        scores, allowed = chunk_scores(c)
        total = total + jnp.sum(jnp.where(allowed, jnp.exp(scores - top[..., None]), 0.0), axis=-1)
    lse = top + jnp.log(total)

    dquery = jnp.zeros((rows, groups, per, head_dim), jnp.float32)
    dks = []
    dvs = []
    for c in range(CHUNKS):
        scores, allowed = chunk_scores(c)
        k_c = k_all[c * width:(c + 1) * width]
        v_c = v_all[c * width:(c + 1) * width]
        prob = jnp.where(allowed, jnp.exp(scores - lse[..., None]), 0.0)
        prob_b = prob.astype(jnp.bfloat16)
        dvalue = jnp.einsum("geij,iged->jgd", prob_b, do_local, preferred_element_type=jnp.float32)
        dprob = jnp.einsum("iged,jgd->geij", do_local, v_c, preferred_element_type=jnp.float32)
        dscore = (prob * (dprob - delta[..., None])).astype(jnp.bfloat16)
        dquery = dquery + jnp.einsum("geij,jgd->iged", dscore, k_c, preferred_element_type=jnp.float32)
        dkey = jnp.einsum("geij,iged->jgd", dscore, q_local, preferred_element_type=jnp.float32)
        dks.append(dkey.reshape(width, kv_width))
        dvs.append(dvalue.reshape(width, kv_width))
    dkv = jnp.concatenate([jnp.concatenate(dks, axis=0), jnp.concatenate(dvs, axis=0)], axis=1)
    dkv = lax.psum_scatter(dkv, "ctx", scatter_dimension=0, tiled=True)
    dkey = dkv[:, :kv_width]
    dvalue = dkv[:, kv_width:]
    grad_query = (scale * dquery).reshape(rows, heads * head_dim).astype(jnp.bfloat16)[None]
    grad_keys = (scale * dkey).astype(jnp.bfloat16)[None]
    grad_values = dvalue.astype(jnp.bfloat16)[None]
    return (grad_query, grad_keys, grad_values)


def solution(mesh):
    return jax.shard_map(
        body,
        mesh=mesh,
        in_specs=(
            P("segment", "ctx", "tp"),
            P("segment", "ctx", "tp"),
            P("segment", "ctx", "tp"),
            P("segment", "ctx", "tp"),
            P("segment", ("ctx", "tp"), None),
            P("segment", None),
        ),
        out_specs=(P("segment", "ctx", "tp"), P("segment", "ctx", "tp"), P("segment", "ctx", "tp")),
        check_vma=False,
    )
```

```python
import jax
import jax.numpy as jnp
from jax import lax
from jax.sharding import PartitionSpec as P

HEAD_DIM = 128
CHUNKS = 4


def passed_along(value, axis, steps):
    count = lax.axis_size(axis)
    pairs = [(source, (source + steps) % count) for source in range(count)]
    return lax.ppermute(value, axis, pairs)


def body(query, keys, values, attn_out, grad_out, block_of):
    rows = query.shape[1]
    kv_width = keys.shape[2]
    head_dim = HEAD_DIM
    groups = kv_width // head_dim
    heads = query.shape[2] // head_dim
    per = heads // groups
    scale = head_dim ** (-0.5)
    half = rows // 2
    order = block_of[0]
    me = lax.axis_index("ctx")
    handed = passed_along(grad_out[0], "segment", -1)
    incoming = lax.all_to_all(handed, "tp", split_axis=1, concat_axis=0, tiled=True)
    q_local = query[0].reshape(rows, groups, per, head_dim)
    do_local = incoming.reshape(rows, groups, per, head_dim)
    delta = jnp.sum(
        attn_out[0].reshape(rows, groups, per, head_dim).astype(jnp.float32)
        * do_local.astype(jnp.float32),
        axis=-1,
    )
    delta = jnp.transpose(delta, (1, 2, 0))

    def place(first, length):
        index = first + jnp.arange(length, dtype=jnp.int32)
        table = (index // half)[:, None] == jnp.arange(order.shape[0], dtype=jnp.int32)[None, :]
        return jnp.sum(jnp.where(table, order[None, :], 0), axis=1) * half + index % half

    q_pos = place(me * rows, rows)

    kv = jnp.concatenate([keys[0], values[0]], axis=1)
    kv_all = lax.all_gather(kv, "ctx", axis=0, tiled=True)
    seq = kv_all.shape[0]
    k_all = kv_all[:, :kv_width].reshape(seq, groups, head_dim)
    v_all = kv_all[:, kv_width:].reshape(seq, groups, head_dim)
    k_pos_all = place(jnp.int32(0), seq)
    width = seq // CHUNKS

    def chunk_scores(c):
        k_c = k_all[c * width:(c + 1) * width]
        scores = scale * jnp.einsum(
            "iged,jgd->geij", q_local, k_c, preferred_element_type=jnp.float32
        )
        allowed = k_pos_all[c * width:(c + 1) * width][None, :] <= q_pos[:, None]
        return scores, allowed

    tops = []
    for c in range(CHUNKS):
        scores, allowed = chunk_scores(c)
        tops.append(jnp.max(jnp.where(allowed, scores, -1e30), axis=-1))
    top = tops[0]
    for t in tops[1:]:
        top = jnp.maximum(top, t)
    total = jnp.zeros_like(top)
    for c in range(CHUNKS):
        scores, allowed = chunk_scores(c)
        total = total + jnp.sum(jnp.where(allowed, jnp.exp(scores - top[..., None]), 0.0), axis=-1)
    lse = top + jnp.log(total)

    dquery = jnp.zeros((rows, groups, per, head_dim), jnp.float32)
    dks = []
    dvs = []
    for c in range(CHUNKS):
        scores, allowed = chunk_scores(c)
        k_c = k_all[c * width:(c + 1) * width]
        v_c = v_all[c * width:(c + 1) * width]
        prob = jnp.where(allowed, jnp.exp(scores - lse[..., None]), 0.0)
        prob_b = prob.astype(jnp.bfloat16)
        dvalue = jnp.einsum("geij,iged->jgd", prob_b, do_local, preferred_element_type=jnp.float32)
        dprob = jnp.einsum("iged,jgd->geij", do_local, v_c, preferred_element_type=jnp.float32)
        dscore = (prob * (dprob - delta[..., None])).astype(jnp.bfloat16)
        dquery = dquery + jnp.einsum("geij,jgd->iged", dscore, k_c, preferred_element_type=jnp.float32)
        dkey = jnp.einsum("geij,iged->jgd", dscore, q_local, preferred_element_type=jnp.float32)
        dks.append(dkey.reshape(width, kv_width))
        dvs.append(dvalue.reshape(width, kv_width))
    dkv = jnp.concatenate([jnp.concatenate(dks, axis=0), jnp.concatenate(dvs, axis=0)], axis=1)
    count = lax.axis_size("ctx")
    dkv = lax.all_to_all(
        dkv.astype(jnp.bfloat16).reshape(count, rows, 2 * kv_width), "ctx", 0, 0, tiled=True
    )
    dkv = jnp.sum(dkv.astype(jnp.float32), axis=0)
    dkey = dkv[:, :kv_width]
    dvalue = dkv[:, kv_width:]
    grad_query = (scale * dquery).reshape(rows, heads * head_dim).astype(jnp.bfloat16)[None]
    grad_keys = (scale * dkey).astype(jnp.bfloat16)[None]
    grad_values = dvalue.astype(jnp.bfloat16)[None]
    return (grad_query, grad_keys, grad_values)


def solution(mesh):
    return jax.shard_map(
        body,
        mesh=mesh,
        in_specs=(
            P("segment", "ctx", "tp"),
            P("segment", "ctx", "tp"),
            P("segment", "ctx", "tp"),
            P("segment", "ctx", "tp"),
            P("segment", ("ctx", "tp"), None),
            P("segment", None),
        ),
        out_specs=(P("segment", "ctx", "tp"), P("segment", "ctx", "tp"), P("segment", "ctx", "tp")),
        check_vma=False,
    )
```

```python
import jax
import jax.numpy as jnp
from jax import lax
from jax.sharding import PartitionSpec as P


HEAD_DIM = 128
CHUNKS = 4


def passed_along(value, axis, steps):
    count = lax.axis_size(axis)
    pairs = [(source, (source + steps) % count) for source in range(count)]
    return lax.ppermute(value, axis, pairs)


def section(query, keys, values, attn_out, grad_out, block_of):
    rows = query.shape[1]
    kv_width = keys.shape[2]
    head_dim = HEAD_DIM
    groups = kv_width // head_dim
    heads = query.shape[2] // head_dim
    per = heads // groups
    scale = head_dim ** (-0.5)
    half = rows // 2
    order = block_of[0]
    me = lax.axis_index("ctx")
    handed = passed_along(grad_out[0], "segment", -1)
    ways = lax.axis_size("tp")
    mine = lax.axis_index("tp")
    width_tp = handed.shape[1] // ways
    pieces = [lax.dynamic_slice_in_dim(handed, mine * width_tp, width_tp, axis=1)]
    for shift in range(1, ways):
        out = lax.dynamic_slice_in_dim(handed, ((mine + shift) % ways) * width_tp, width_tp, axis=1)
        pieces.append(passed_along(out, "tp", shift))
    stacked = jnp.stack(pieces[::-1], axis=0)
    incoming = jnp.roll(stacked, mine + 1, axis=0).reshape(ways * handed.shape[0], width_tp)
    q_local = query[0].reshape(rows, groups, per, head_dim)
    do_local = incoming.reshape(rows, groups, per, head_dim)
    delta = jnp.sum(
        attn_out[0].reshape(rows, groups, per, head_dim).astype(jnp.float32)
        * do_local.astype(jnp.float32),
        axis=-1,
    )
    delta = jnp.transpose(delta, (1, 2, 0))

    def place(first, length):
        index = first + jnp.arange(length, dtype=jnp.int32)
        table = (index // half)[:, None] == jnp.arange(order.shape[0], dtype=jnp.int32)[None, :]
        return jnp.sum(jnp.where(table, order[None, :], 0), axis=1) * half + index % half

    q_pos = place(me * rows, rows)

    kv = jnp.concatenate([keys[0], values[0]], axis=1)
    count = lax.axis_size("ctx")
    kv_all = lax.all_to_all(
        jnp.broadcast_to(kv[None], (count,) + kv.shape), "ctx", 0, 0, tiled=True
    ).reshape(count * rows, 2 * kv_width)
    seq = kv_all.shape[0]
    k_all = kv_all[:, :kv_width].reshape(seq, groups, head_dim)
    v_all = kv_all[:, kv_width:].reshape(seq, groups, head_dim)
    k_pos_all = place(jnp.int32(0), seq)
    width = seq // CHUNKS

    def chunk_scores(c):
        k_c = k_all[c * width:(c + 1) * width]
        scores = scale * jnp.einsum(
            "iged,jgd->geij", q_local, k_c, preferred_element_type=jnp.float32
        )
        allowed = k_pos_all[c * width:(c + 1) * width][None, :] <= q_pos[:, None]
        return scores, allowed

    tops = []
    for c in range(CHUNKS):
        scores, allowed = chunk_scores(c)
        tops.append(jnp.max(jnp.where(allowed, scores, -1e30), axis=-1))
    top = tops[0]
    for t in tops[1:]:
        top = jnp.maximum(top, t)
    total = jnp.zeros_like(top)
    for c in range(CHUNKS):
        scores, allowed = chunk_scores(c)
        total = total + jnp.sum(jnp.where(allowed, jnp.exp(scores - top[..., None]), 0.0), axis=-1)
    lse = top + jnp.log(total)

    dquery = jnp.zeros((rows, groups, per, head_dim), jnp.float32)
    dks = []
    dvs = []
    for c in range(CHUNKS):
        scores, allowed = chunk_scores(c)
        k_c = k_all[c * width:(c + 1) * width]
        v_c = v_all[c * width:(c + 1) * width]
        prob = jnp.where(allowed, jnp.exp(scores - lse[..., None]), 0.0)
        prob_b = prob.astype(jnp.bfloat16)
        dvalue = jnp.einsum("geij,iged->jgd", prob_b, do_local, preferred_element_type=jnp.float32)
        dprob = jnp.einsum("iged,jgd->geij", do_local, v_c, preferred_element_type=jnp.float32)
        dscore = (prob * (dprob - delta[..., None])).astype(jnp.bfloat16)
        dquery = dquery + jnp.einsum("geij,jgd->iged", dscore, k_c, preferred_element_type=jnp.float32)
        dkey = jnp.einsum("geij,iged->jgd", dscore, q_local, preferred_element_type=jnp.float32)
        dks.append(dkey.reshape(width, kv_width))
        dvs.append(dvalue.reshape(width, kv_width))
    dkv = jnp.concatenate([jnp.concatenate(dks, axis=0), jnp.concatenate(dvs, axis=0)], axis=1)
    count = lax.axis_size("ctx")
    dkv = lax.all_to_all(
        dkv.astype(jnp.bfloat16).reshape(count, rows, 2 * kv_width), "ctx", 0, 0, tiled=True
    )
    dkv = jnp.sum(dkv.astype(jnp.float32), axis=0)
    dkey = dkv[:, :kv_width]
    dvalue = dkv[:, kv_width:]
    grad_query = (scale * dquery).reshape(rows, heads * head_dim).astype(jnp.bfloat16)[None]
    grad_keys = (scale * dkey).astype(jnp.bfloat16)[None]
    grad_values = dvalue.astype(jnp.bfloat16)[None]
    return (grad_query, grad_keys, grad_values)


def solution(mesh):
    return jax.shard_map(
        section,
        mesh=mesh,
        in_specs=(
            P("segment", "ctx", "tp"),
            P("segment", "ctx", "tp"),
            P("segment", "ctx", "tp"),
            P("segment", "ctx", "tp"),
            P("segment", ("ctx", "tp"), None),
            P("segment", None),
        ),
        out_specs=(P("segment", "ctx", "tp"), P("segment", "ctx", "tp"), P("segment", "ctx", "tp")),
        check_vma=False,
    )
```

```python
import jax
import jax.numpy as jnp
from jax import lax
from jax.sharding import PartitionSpec as P


HEAD_DIM = 128
CHUNKS = 4


def passed_along(value, axis, steps):
    count = lax.axis_size(axis)
    pairs = [(source, (source + steps) % count) for source in range(count)]
    return lax.ppermute(value, axis, pairs)


def section(query, keys, values, attn_out, grad_out, block_of):
    rows = query.shape[1]
    kv_width = keys.shape[2]
    head_dim = HEAD_DIM
    groups = kv_width // head_dim
    heads = query.shape[2] // head_dim
    per = heads // groups
    scale = head_dim ** (-0.5)
    half = rows // 2
    order = block_of[0]
    me = lax.axis_index("ctx")
    handed = passed_along(grad_out[0], "segment", -1)
    ways = lax.axis_size("tp")
    mine = lax.axis_index("tp")
    width_tp = handed.shape[1] // ways
    pieces = [lax.dynamic_slice_in_dim(handed, mine * width_tp, width_tp, axis=1)]
    for shift in range(1, ways):
        out = lax.dynamic_slice_in_dim(handed, ((mine + shift) % ways) * width_tp, width_tp, axis=1)
        pieces.append(passed_along(out, "tp", shift))
    stacked = jnp.stack(pieces[::-1], axis=0)
    incoming = jnp.roll(stacked, mine + 1, axis=0).reshape(ways * handed.shape[0], width_tp)
    q_local = query[0].reshape(rows, groups, per, head_dim)
    do_local = incoming.reshape(rows, groups, per, head_dim)
    delta = jnp.sum(
        attn_out[0].reshape(rows, groups, per, head_dim).astype(jnp.float32)
        * do_local.astype(jnp.float32),
        axis=-1,
    )
    delta = jnp.transpose(delta, (1, 2, 0))

    def place(first, length):
        index = first + jnp.arange(length, dtype=jnp.int32)
        table = (index // half)[:, None] == jnp.arange(order.shape[0], dtype=jnp.int32)[None, :]
        return jnp.sum(jnp.where(table, order[None, :], 0), axis=1) * half + index % half

    q_pos = place(me * rows, rows)

    kv = jnp.concatenate([keys[0], values[0]], axis=1)
    count = lax.axis_size("ctx")
    kv_all = lax.all_to_all(
        jnp.broadcast_to(kv[None], (count,) + kv.shape), "ctx", 0, 0, tiled=True
    ).reshape(count * rows, 2 * kv_width)
    seq = kv_all.shape[0]
    k_all = kv_all[:, :kv_width].reshape(seq, groups, head_dim)
    v_all = kv_all[:, kv_width:].reshape(seq, groups, head_dim)
    k_pos_all = place(jnp.int32(0), seq)
    width = seq // CHUNKS
    q_g = jnp.transpose(q_local, (1, 2, 0, 3)).reshape(groups, per * rows, head_dim)
    do_g = jnp.transpose(do_local, (1, 2, 0, 3)).reshape(groups, per * rows, head_dim)
    delta_g = delta.reshape(groups, per * rows)
    q_pos_m = jnp.tile(q_pos, per)

    def chunk_scores(c):
        k_c = k_all[c * width:(c + 1) * width]
        scores = scale * jnp.einsum("gmd,jgd->gmj", q_g, k_c, preferred_element_type=jnp.float32)
        allowed = k_pos_all[c * width:(c + 1) * width][None, :] <= q_pos_m[:, None]
        return scores, allowed

    tops = []
    for c in range(CHUNKS):
        scores, allowed = chunk_scores(c)
        tops.append(jnp.max(jnp.where(allowed, scores, -1e30), axis=-1))
    top = tops[0]
    for t in tops[1:]:
        top = jnp.maximum(top, t)
    total = jnp.zeros_like(top)
    for c in range(CHUNKS):
        scores, allowed = chunk_scores(c)
        total = total + jnp.sum(jnp.where(allowed, jnp.exp(scores - top[..., None]), 0.0), axis=-1)
    lse = top + jnp.log(total)

    dquery_g = jnp.zeros((groups, per * rows, head_dim), jnp.float32)
    dks = []
    dvs = []
    for c in range(CHUNKS):
        scores, allowed = chunk_scores(c)
        k_c = k_all[c * width:(c + 1) * width]
        v_c = v_all[c * width:(c + 1) * width]
        prob = jnp.where(allowed, jnp.exp(scores - lse[..., None]), 0.0)
        prob_b = prob.astype(jnp.bfloat16)
        dvalue = jnp.einsum("gmj,gmd->jgd", prob_b, do_g, preferred_element_type=jnp.float32)
        dprob = jnp.einsum("gmd,jgd->gmj", do_g, v_c, preferred_element_type=jnp.float32)
        dscore = (prob * (dprob - delta_g[..., None])).astype(jnp.bfloat16)
        dquery_g = dquery_g + jnp.einsum("gmj,jgd->gmd", dscore, k_c, preferred_element_type=jnp.float32)
        dkey = jnp.einsum("gmj,gmd->jgd", dscore, q_g, preferred_element_type=jnp.float32)
        dks.append(dkey.reshape(width, kv_width))
        dvs.append(dvalue.reshape(width, kv_width))
    dquery = jnp.transpose(dquery_g.reshape(groups, per, rows, head_dim), (2, 0, 1, 3))
    dkv = jnp.concatenate([jnp.concatenate(dks, axis=0), jnp.concatenate(dvs, axis=0)], axis=1)
    count = lax.axis_size("ctx")
    dkv = lax.all_to_all(
        dkv.astype(jnp.bfloat16).reshape(count, rows, 2 * kv_width), "ctx", 0, 0, tiled=True
    )
    dkv = jnp.sum(dkv.astype(jnp.float32), axis=0)
    dkey = dkv[:, :kv_width]
    dvalue = dkv[:, kv_width:]
    grad_query = (scale * dquery).reshape(rows, heads * head_dim).astype(jnp.bfloat16)[None]
    grad_keys = (scale * dkey).astype(jnp.bfloat16)[None]
    grad_values = dvalue.astype(jnp.bfloat16)[None]
    return (grad_query, grad_keys, grad_values)


def solution(mesh):
    return jax.shard_map(
        section,
        mesh=mesh,
        in_specs=(
            P("segment", "ctx", "tp"),
            P("segment", "ctx", "tp"),
            P("segment", "ctx", "tp"),
            P("segment", "ctx", "tp"),
            P("segment", ("ctx", "tp"), None),
            P("segment", None),
        ),
        out_specs=(P("segment", "ctx", "tp"), P("segment", "ctx", "tp"), P("segment", "ctx", "tp")),
        check_vma=False,
    )
```

```python
import jax
import jax.numpy as jnp
from jax import lax
from jax.sharding import PartitionSpec as P


HEAD_DIM = 128
CHUNKS = 1


def passed_along(value, axis, steps):
    count = lax.axis_size(axis)
    pairs = [(source, (source + steps) % count) for source in range(count)]
    return lax.ppermute(value, axis, pairs)


def section(query, keys, values, attn_out, grad_out, block_of):
    rows = query.shape[1]
    kv_width = keys.shape[2]
    head_dim = HEAD_DIM
    groups = kv_width // head_dim
    heads = query.shape[2] // head_dim
    per = heads // groups
    scale = head_dim ** (-0.5)
    half = rows // 2
    order = block_of[0]
    me = lax.axis_index("ctx")
    handed = passed_along(grad_out[0], "segment", -1)
    ways = lax.axis_size("tp")
    mine = lax.axis_index("tp")
    width_tp = handed.shape[1] // ways
    pieces = [lax.dynamic_slice_in_dim(handed, mine * width_tp, width_tp, axis=1)]
    for shift in range(1, ways):
        out = lax.dynamic_slice_in_dim(handed, ((mine + shift) % ways) * width_tp, width_tp, axis=1)
        pieces.append(passed_along(out, "tp", shift))
    stacked = jnp.stack(pieces[::-1], axis=0)
    incoming = jnp.roll(stacked, mine + 1, axis=0).reshape(ways * handed.shape[0], width_tp)
    q_local = query[0].reshape(rows, groups, per, head_dim)
    do_local = incoming.reshape(rows, groups, per, head_dim)
    delta = jnp.sum(
        attn_out[0].reshape(rows, groups, per, head_dim).astype(jnp.float32)
        * do_local.astype(jnp.float32),
        axis=-1,
    )
    delta = jnp.transpose(delta, (1, 2, 0))

    def place(first, length):
        index = first + jnp.arange(length, dtype=jnp.int32)
        table = (index // half)[:, None] == jnp.arange(order.shape[0], dtype=jnp.int32)[None, :]
        return jnp.sum(jnp.where(table, order[None, :], 0), axis=1) * half + index % half

    q_pos = place(me * rows, rows)

    kv = jnp.concatenate([keys[0], values[0]], axis=1)
    count = lax.axis_size("ctx")
    kv_all = lax.all_to_all(
        jnp.broadcast_to(kv[None], (count,) + kv.shape), "ctx", 0, 0, tiled=True
    ).reshape(count * rows, 2 * kv_width)
    seq = kv_all.shape[0]
    k_all = kv_all[:, :kv_width].reshape(seq, groups, head_dim)
    v_all = kv_all[:, kv_width:].reshape(seq, groups, head_dim)
    k_pos_all = place(jnp.int32(0), seq)
    width = seq // CHUNKS
    q_g = jnp.transpose(q_local, (1, 2, 0, 3)).reshape(groups, per * rows, head_dim)
    do_g = jnp.transpose(do_local, (1, 2, 0, 3)).reshape(groups, per * rows, head_dim)
    delta_g = delta.reshape(groups, per * rows)
    q_pos_m = jnp.tile(q_pos, per)

    def chunk_scores(c):
        k_c = k_all[c * width:(c + 1) * width]
        scores = scale * jnp.einsum("gmd,jgd->gmj", q_g, k_c, preferred_element_type=jnp.float32)
        allowed = k_pos_all[c * width:(c + 1) * width][None, :] <= q_pos_m[:, None]
        return scores, allowed

    tops = []
    sums = []
    for c in range(CHUNKS):
        scores, allowed = chunk_scores(c)
        chunk_top = jnp.max(jnp.where(allowed, scores, -1e30), axis=-1)
        tops.append(chunk_top)
        sums.append(jnp.sum(jnp.where(allowed, jnp.exp(scores - chunk_top[..., None]), 0.0), axis=-1))
    top = tops[0]
    for t in tops[1:]:
        top = jnp.maximum(top, t)
    total = jnp.zeros_like(top)
    for chunk_top, chunk_sum in zip(tops, sums):
        total = total + chunk_sum * jnp.exp(chunk_top - top)
    lse = top + jnp.log(total)

    dquery_g = jnp.zeros((groups, per * rows, head_dim), jnp.float32)
    dks = []
    dvs = []
    for c in range(CHUNKS):
        scores, allowed = chunk_scores(c)
        k_c = k_all[c * width:(c + 1) * width]
        v_c = v_all[c * width:(c + 1) * width]
        prob = jnp.where(allowed, jnp.exp(scores - lse[..., None]), 0.0)
        prob_b = prob.astype(jnp.bfloat16)
        dvalue = jnp.einsum("gmj,gmd->jgd", prob_b, do_g, preferred_element_type=jnp.float32)
        dprob = jnp.einsum("gmd,jgd->gmj", do_g, v_c, preferred_element_type=jnp.float32)
        dscore = (prob * (dprob - delta_g[..., None])).astype(jnp.bfloat16)
        dquery_g = dquery_g + jnp.einsum("gmj,jgd->gmd", dscore, k_c, preferred_element_type=jnp.float32)
        dkey = jnp.einsum("gmj,gmd->jgd", dscore, q_g, preferred_element_type=jnp.float32)
        dks.append(dkey.reshape(width, kv_width))
        dvs.append(dvalue.reshape(width, kv_width))
    dquery = jnp.transpose(dquery_g.reshape(groups, per, rows, head_dim), (2, 0, 1, 3))
    dkv = jnp.concatenate([jnp.concatenate(dks, axis=0), jnp.concatenate(dvs, axis=0)], axis=1)
    count = lax.axis_size("ctx")
    dkv = lax.all_to_all(
        dkv.astype(jnp.bfloat16).reshape(count, rows, 2 * kv_width), "ctx", 0, 0, tiled=True
    )
    dkv = jnp.sum(dkv.astype(jnp.float32), axis=0)
    dkey = dkv[:, :kv_width]
    dvalue = dkv[:, kv_width:]
    grad_query = (scale * dquery).reshape(rows, heads * head_dim).astype(jnp.bfloat16)[None]
    grad_keys = (scale * dkey).astype(jnp.bfloat16)[None]
    grad_values = dvalue.astype(jnp.bfloat16)[None]
    return (grad_query, grad_keys, grad_values)


def solution(mesh):
    return jax.shard_map(
        section,
        mesh=mesh,
        in_specs=(
            P("segment", "ctx", "tp"),
            P("segment", "ctx", "tp"),
            P("segment", "ctx", "tp"),
            P("segment", "ctx", "tp"),
            P("segment", ("ctx", "tp"), None),
            P("segment", None),
        ),
        out_specs=(P("segment", "ctx", "tp"), P("segment", "ctx", "tp"), P("segment", "ctx", "tp")),
        check_vma=False,
    )
```

```python
import jax
import jax.numpy as jnp
from jax import lax
from jax.sharding import PartitionSpec as P


HEAD_DIM = 128
CHUNKS = 2


def passed_along(value, axis, steps):
    count = lax.axis_size(axis)
    pairs = [(source, (source + steps) % count) for source in range(count)]
    return lax.ppermute(value, axis, pairs)


def section(query, keys, values, attn_out, grad_out, block_of):
    rows = query.shape[1]
    kv_width = keys.shape[2]
    head_dim = HEAD_DIM
    groups = kv_width // head_dim
    heads = query.shape[2] // head_dim
    per = heads // groups
    scale = head_dim ** (-0.5)
    half = rows // 2
    order = block_of[0]
    me = lax.axis_index("ctx")
    handed = passed_along(grad_out[0], "segment", -1)
    ways = lax.axis_size("tp")
    mine = lax.axis_index("tp")
    width_tp = handed.shape[1] // ways
    pieces = [lax.dynamic_slice_in_dim(handed, mine * width_tp, width_tp, axis=1)]
    for shift in range(1, ways):
        out = lax.dynamic_slice_in_dim(handed, ((mine + shift) % ways) * width_tp, width_tp, axis=1)
        pieces.append(passed_along(out, "tp", shift))
    stacked = jnp.stack(pieces[::-1], axis=0)
    incoming = jnp.roll(stacked, mine + 1, axis=0).reshape(ways * handed.shape[0], width_tp)
    q_local = query[0].reshape(rows, groups, per, head_dim)
    do_local = incoming.reshape(rows, groups, per, head_dim)
    delta = jnp.sum(
        attn_out[0].reshape(rows, groups, per, head_dim).astype(jnp.float32)
        * do_local.astype(jnp.float32),
        axis=-1,
    )
    delta = jnp.transpose(delta, (1, 2, 0))

    def place(first, length):
        index = first + jnp.arange(length, dtype=jnp.int32)
        table = (index // half)[:, None] == jnp.arange(order.shape[0], dtype=jnp.int32)[None, :]
        return jnp.sum(jnp.where(table, order[None, :], 0), axis=1) * half + index % half

    q_pos = place(me * rows, rows)

    kv = jnp.concatenate([keys[0], values[0]], axis=1)
    count = lax.axis_size("ctx")
    kv_all = lax.all_to_all(
        jnp.broadcast_to(kv[None], (count,) + kv.shape), "ctx", 0, 0, tiled=True
    ).reshape(count * rows, 2 * kv_width)
    seq = kv_all.shape[0]
    k_all = kv_all[:, :kv_width].reshape(seq, groups, head_dim)
    v_all = kv_all[:, kv_width:].reshape(seq, groups, head_dim)
    k_pos_all = place(jnp.int32(0), seq)
    width = seq // CHUNKS
    q_g = jnp.transpose(q_local, (1, 2, 0, 3)).reshape(groups, per * rows, head_dim)
    do_g = jnp.transpose(do_local, (1, 2, 0, 3)).reshape(groups, per * rows, head_dim)
    delta_g = delta.reshape(groups, per * rows)
    q_pos_m = jnp.tile(q_pos, per)

    def chunk_scores(c):
        k_c = k_all[c * width:(c + 1) * width]
        scores = scale * jnp.einsum("gmd,jgd->gmj", q_g, k_c, preferred_element_type=jnp.float32)
        allowed = k_pos_all[c * width:(c + 1) * width][None, :] <= q_pos_m[:, None]
        return scores, allowed

    tops = []
    sums = []
    terms = []
    for c in range(CHUNKS):
        scores, allowed = chunk_scores(c)
        chunk_top = jnp.max(jnp.where(allowed, scores, -1e30), axis=-1)
        tops.append(chunk_top)
        term = jnp.where(allowed, jnp.exp(scores - chunk_top[..., None]), 0.0)
        terms.append(term)
        sums.append(jnp.sum(term, axis=-1))
    top = tops[0]
    for t in tops[1:]:
        top = jnp.maximum(top, t)
    total = jnp.zeros_like(top)
    for chunk_top, chunk_sum in zip(tops, sums):
        total = total + chunk_sum * jnp.exp(chunk_top - top)
    lse = top + jnp.log(total)

    dquery_g = jnp.zeros((groups, per * rows, head_dim), jnp.float32)
    dks = []
    dvs = []
    for c in range(CHUNKS):
        k_c = k_all[c * width:(c + 1) * width]
        v_c = v_all[c * width:(c + 1) * width]
        prob = terms[c] * jnp.exp(tops[c] - lse)[..., None]
        prob_b = prob.astype(jnp.bfloat16)
        dvalue = jnp.einsum("gmj,gmd->jgd", prob_b, do_g, preferred_element_type=jnp.float32)
        dprob = jnp.einsum("gmd,jgd->gmj", do_g, v_c, preferred_element_type=jnp.float32)
        dscore = (prob * (dprob - delta_g[..., None])).astype(jnp.bfloat16)
        dquery_g = dquery_g + jnp.einsum("gmj,jgd->gmd", dscore, k_c, preferred_element_type=jnp.float32)
        dkey = jnp.einsum("gmj,gmd->jgd", dscore, q_g, preferred_element_type=jnp.float32)
        dks.append(dkey.reshape(width, kv_width))
        dvs.append(dvalue.reshape(width, kv_width))
    dquery = jnp.transpose(dquery_g.reshape(groups, per, rows, head_dim), (2, 0, 1, 3))
    dkv = jnp.concatenate([jnp.concatenate(dks, axis=0), jnp.concatenate(dvs, axis=0)], axis=1)
    count = lax.axis_size("ctx")
    dkv = lax.all_to_all(
        dkv.astype(jnp.bfloat16).reshape(count, rows, 2 * kv_width), "ctx", 0, 0, tiled=True
    )
    dkv = jnp.sum(dkv.astype(jnp.float32), axis=0)
    dkey = dkv[:, :kv_width]
    dvalue = dkv[:, kv_width:]
    grad_query = (scale * dquery).reshape(rows, heads * head_dim).astype(jnp.bfloat16)[None]
    grad_keys = (scale * dkey).astype(jnp.bfloat16)[None]
    grad_values = dvalue.astype(jnp.bfloat16)[None]
    return (grad_query, grad_keys, grad_values)


def solution(mesh):
    return jax.shard_map(
        section,
        mesh=mesh,
        in_specs=(
            P("segment", "ctx", "tp"),
            P("segment", "ctx", "tp"),
            P("segment", "ctx", "tp"),
            P("segment", "ctx", "tp"),
            P("segment", ("ctx", "tp"), None),
            P("segment", None),
        ),
        out_specs=(P("segment", "ctx", "tp"), P("segment", "ctx", "tp"), P("segment", "ctx", "tp")),
        check_vma=False,
    )
```
